512 devices in a mesh: dp: 64 (over z, x_lo, core), tensor: 8 (over y, x_hi).
Axes of the slice: x: 4 (x_hi: 2, x_lo: 2; x = x_hi * 2 + x_lo), y: 4, z: 16, core: 2. Of those that a mesh axis runs over, the one named last changes fastest.
Arguments:
- hidden_in: bfloat16 [16384, 4096], P(('dp', 'tensor')), may hold values from -12 to 12
- norm_gain: bfloat16 [4096], replicated, may hold values from 0.5 to 1.5
- w_query: bfloat16 [4096, 4096], P('dp', 'tensor'), may hold values from -0.11328125 to 0.11328125
- w_key: bfloat16 [4096, 1024], P('dp', 'tensor'), may hold values from -0.11328125 to 0.11328125
- w_value: bfloat16 [4096, 1024], P('dp', 'tensor'), may hold values from -0.09375 to 0.09375
- w_out: bfloat16 [4096, 4096], P('tensor', 'dp'), may hold values from -0.09375 to 0.09375
- segment: int32 [16384], P('dp'), may hold values from -1 to 1, as said below
Outputs:
- hidden_out: bfloat16 [16384, 4096], P(('dp', 'tensor'))
- kv_cache: bfloat16 [16384, 8, 256], P('dp', 'tensor')
The draws below stay inside these ranges and needn't reach their ends.
Inputs may be any that keep to these rules, and one draw needn't show every extreme that they name: `segment`: within each pack of 256 rows, prompts are numbered from 0 in order and each starts at a multiple of 128; a prompt's last tile may end in rows of -1, and whole tiles of -1 may only follow the last prompt of a pack; the first tile of every pack holds a prompt; in every draw some pack has no tile of -1 only and holds one prompt a tile.
All inputs are finite; a program needn't handle non-finite values.
Results may differ from the reference program's by a relative error of at most 0.0085.
Values may be sent and summed in bfloat16 or wider, within the bound.
No kernel may reach another device: no remote copies, remote signals or barrier semaphores. Data moves between devices by JAX's collectives and lax.ppermute only.
A program may use at most 64 MiB of HBM per device.

```python
import jax
import jax.numpy as jnp
from jax import lax

D = 4096
HQ = 32
KVH = 8
HEAD = 128
TILE = 128
PACK = 256
TOKENS = 16384
N_DP = 64
N_TENSOR = 8


def draw_hidden_in(key, part):
    own_key = jax.random.fold_in(key, 1)
    values = jnp.clip(jax.random.normal(own_key, (TOKENS, D), jnp.float32), -6.0, 6.0)
    return values.astype(jnp.bfloat16)


def draw_w_query(key, part):
    values = jnp.clip(jax.random.normal(jax.random.fold_in(key, 2), (D, HQ * HEAD), jnp.float32), -6.0, 6.0) * D ** (-0.5)
    return values.astype(jnp.bfloat16)


def draw_w_key(key, part):
    values = jnp.clip(jax.random.normal(jax.random.fold_in(key, 3), (D, KVH * HEAD), jnp.float32), -6.0, 6.0) * D ** (-0.5)
    return values.astype(jnp.bfloat16)


def draw_segment(key, part):
    shards = TOKENS // PACK
    tile_count = PACK // TILE
    key_full, key_live, key_start, key_pad = jax.random.split(jax.random.fold_in(key, 4), 4)
    fullest = jax.random.randint(key_full, (), 0, shards)
    is_fullest = jnp.arange(shards) == fullest
    live_tiles = jax.random.randint(key_live, (shards,), 1, tile_count + 1)
    live_tiles = jnp.where(is_fullest, tile_count, live_tiles)
    starts = jax.random.randint(key_start, (shards, tile_count), 0, 2)
    starts = jnp.where(is_fullest[:, None], 1, starts)
    starts = starts.at[:, 0].set(1)
    tile_index = jnp.arange(tile_count)[None, :]
    tile_alive = tile_index < live_tiles[:, None]
    tile_segment = jnp.cumsum(starts, axis=1) - 1
    next_start = jnp.concatenate([starts[:, 1:], jnp.ones((shards, 1), jnp.int32)], axis=1)
    last_tile = (next_start == 1) | (tile_index == live_tiles[:, None] - 1)
    pad_length = jax.random.randint(key_pad, (shards, tile_count), 0, TILE)
    offset = jnp.arange(TILE)[None, None, :]
    is_padding = last_tile[:, :, None] & (offset >= TILE - pad_length[:, :, None])
    segment_ids = jnp.where(tile_alive[:, :, None] & jnp.logical_not(is_padding), tile_segment[:, :, None], -1)
    return segment_ids.reshape(TOKENS).astype(jnp.int32)


def level_of(key, dims, cuts, low, top_value):
    def one(axis_at, blocks):
        heights = jax.random.uniform(jax.random.fold_in(jax.random.fold_in(key, 6), axis_at), (blocks,), jnp.float32, low / len(cuts), top_value / len(cuts))
        return jnp.repeat(jnp.exp(heights), dims[axis_at] // blocks).reshape((-1,) + (1,) * (len(dims) - axis_at - 1))

    gain = one(*cuts[0])
    for cut in cuts[1:]:
        gain = gain * one(*cut)
    return gain


def noise(key, dims, width, limit, cuts=(), kind=jnp.bfloat16):
    drawn = width * jax.random.normal(key, dims, jnp.float32)
    if cuts:
        drawn = drawn * level_of(key, dims, cuts, -0.22, 0.18)
    return jnp.clip(drawn, -limit, limit).astype(kind)


def setup_inputs(seed: int = 0) -> dict:
    key_of = jax.random.split(jax.random.key(seed), 8)
    hidden_in = draw_hidden_in(jax.random.fold_in(key_of[7], 71), 0)
    norm_gain = jnp.clip(1.0 + 0.1 * jax.random.normal(key_of[1], (D,), jnp.float32), 0.5, 1.5).astype(jnp.bfloat16)
    w_query = draw_w_query(jax.random.fold_in(key_of[7], 71), 0)
    w_key = draw_w_key(jax.random.fold_in(key_of[7], 71), 0)
    w_value = noise(key_of[4], (D, KVH * HEAD), D ** -0.5, 0.09375, ((0, 64), (1, 8)))
    w_out = noise(key_of[5], (HQ * HEAD, D), (HQ * HEAD) ** -0.5, 0.09375, ((0, 8), (1, 64)))
    segment = draw_segment(jax.random.fold_in(key_of[7], 71), 0)
    return {"hidden_in": hidden_in, "norm_gain": norm_gain, "w_query": w_query, "w_key": w_key, "w_value": w_value, "w_out": w_out, "segment": segment}


rope_theta = 500000.0
norm_epsilon = 1e-05

def inverse_frequency(head_width):
    exponent = jnp.arange(0, head_width, 2).astype(jnp.float32) / head_width
    base_freq = rope_theta ** (-exponent)
    wavelength = 2.0 * jnp.pi / base_freq
    smooth = (8192.0 / wavelength - 1.0) / 3.0
    blended = (1.0 - smooth) * base_freq / 8.0 + smooth * base_freq
    return jnp.where(wavelength < 2048.0, base_freq, jnp.where(wavelength > 8192.0, base_freq / 8.0, blended))

def positions_of(segment):
    row_index = jnp.arange(segment.shape[0], dtype=jnp.int32)
    changed = jnp.concatenate([jnp.ones((1,), dtype=bool), segment[1:] != segment[:-1]])
    begins = lax.cummax(jnp.where(changed, row_index, 0), axis=0)
    return row_index - begins

def rotate(vectors, position):
    head_width = vectors.shape[-1]
    half_width = head_width // 2
    angles = position.astype(jnp.float32)[:, None] * inverse_frequency(head_width)[None, :]
    cosine = jnp.concatenate([jnp.cos(angles), jnp.cos(angles)], axis=-1)[:, None, :]
    sine_table = jnp.concatenate([jnp.sin(angles), jnp.sin(angles)], axis=-1)[:, None, :]
    turned = jnp.concatenate([-vectors[..., half_width:], vectors[..., :half_width]], axis=-1)
    return vectors * cosine + turned * sine_table

def rms_normed(rows_float, norm_gain):
    mean_square = lax.optimization_barrier(jnp.mean(rows_float * rows_float, axis=-1, keepdims=True))
    return (rows_float * lax.rsqrt(mean_square + norm_epsilon) * norm_gain.astype(jnp.float32)).astype(jnp.bfloat16)

def visible_pairs(segment, first_key, key_count):
    row_index = jnp.arange(segment.shape[0], dtype=jnp.int32)
    key_index = first_key + jnp.arange(key_count, dtype=jnp.int32)
    key_segment = lax.dynamic_slice_in_dim(segment, first_key, key_count, 0)
    same_segment = (segment[:, None] == key_segment[None, :]) & (segment[:, None] >= 0)
    causal = key_index[None, :] <= row_index[:, None]
    return same_segment & causal | (key_index[None, :] == row_index[:, None])

def reference(hidden_in, norm_gain, w_query, w_key, w_value, w_out, segment):
    group_size = HQ // KVH
    score_scale = HEAD ** (-0.5)
    per_group = HQ * HEAD // N_TENSOR
    out_float = w_out.astype(jnp.float32).reshape(N_TENSOR, per_group, D)

    def one_pack(packed):
        row_block, pack_segment = packed
        rows_float = row_block.astype(jnp.float32)
        normed = rms_normed(rows_float, norm_gain)
        position = positions_of(pack_segment)
        query_raw = jnp.dot(normed, w_query, preferred_element_type=jnp.float32).reshape(PACK, HQ, HEAD)
        key_raw = jnp.dot(normed, w_key, preferred_element_type=jnp.float32).reshape(PACK, KVH, HEAD)
        value_raw = jnp.dot(normed, w_value, preferred_element_type=jnp.float32).reshape(PACK, KVH, HEAD)
        query_rows = rotate(query_raw, position).astype(jnp.bfloat16)
        key_rows = rotate(key_raw, position).astype(jnp.bfloat16)
        value_rows = value_raw.astype(jnp.bfloat16)
        cache_rows = jnp.concatenate([key_rows, value_rows], axis=-1)
        query_float = query_rows.astype(jnp.float32).reshape(PACK, KVH, group_size, HEAD)
        scores = jnp.einsum('skgh,tkh->kgst', query_float, key_rows.astype(jnp.float32)) * score_scale
        allowed = visible_pairs(pack_segment, 0, PACK)
        scores = jnp.where(allowed, scores, -jnp.inf)
        row_max = lax.optimization_barrier(jnp.max(scores, axis=-1, keepdims=True))
        weight = jnp.exp(scores - row_max)
        weight_sum = lax.optimization_barrier(jnp.sum(weight, axis=-1))
        weight_low = lax.optimization_barrier(weight.astype(jnp.bfloat16))
        mixed_rows = jnp.einsum('kgst,tkh->kgsh', weight_low.astype(jnp.float32), value_rows.astype(jnp.float32)) / weight_sum[..., None]
        attended = jnp.transpose(mixed_rows, (2, 0, 1, 3)).astype(jnp.bfloat16).reshape(PACK, HQ * HEAD)
        grouped = attended.astype(jnp.float32).reshape(PACK, N_TENSOR, per_group)
        partial_sums = jnp.einsum('sgc,gcd->gsd', grouped, out_float)
        partial_low = lax.optimization_barrier(partial_sums.astype(jnp.bfloat16))
        hidden_rows = (lax.optimization_barrier(jnp.sum(partial_low.astype(jnp.float32), axis=0)) + rows_float).astype(jnp.bfloat16)
        return (hidden_rows, cache_rows)
    hidden_out, cache_out = lax.map(one_pack, (hidden_in.reshape(N_DP, PACK, D), segment.reshape(N_DP, PACK)))
    return (hidden_out.reshape(PACK * N_DP, D), cache_out.reshape(PACK * N_DP, KVH, 2 * HEAD))
```

```python
import jax
import jax.numpy as jnp
from jax import lax
from jax.sharding import PartitionSpec as P

HEAD = 128


rope_theta = 500000.0
norm_epsilon = 1e-05


def inverse_frequency(head_width):
    exponent = jnp.arange(0, head_width, 2).astype(jnp.float32) / head_width
    base_freq = rope_theta ** (-exponent)
    wavelength = 2.0 * jnp.pi / base_freq
    smooth = (8192.0 / wavelength - 1.0) / 3.0
    blended = (1.0 - smooth) * base_freq / 8.0 + smooth * base_freq
    return jnp.where(
        wavelength < 2048.0, base_freq, jnp.where(wavelength > 8192.0, base_freq / 8.0, blended)
    )


def positions_of(segment):
    row_index = jnp.arange(segment.shape[0], dtype=jnp.int32)
    changed = jnp.concatenate([jnp.ones((1,), dtype=bool), segment[1:] != segment[:-1]])
    begins = lax.cummax(jnp.where(changed, row_index, 0), axis=0)
    return row_index - begins


def rotate(vectors, position):
    head_width = vectors.shape[-1]
    half_width = head_width // 2
    angles = position.astype(jnp.float32)[:, None] * inverse_frequency(head_width)[None, :]
    cosine = jnp.concatenate([jnp.cos(angles), jnp.cos(angles)], axis=-1)[:, None, :]
    sine_table = jnp.concatenate([jnp.sin(angles), jnp.sin(angles)], axis=-1)[:, None, :]
    turned = jnp.concatenate([-vectors[..., half_width:], vectors[..., :half_width]], axis=-1)
    return vectors * cosine + turned * sine_table


def rms_normed(rows_float, norm_gain):
    mean_square = jnp.mean(rows_float * rows_float, axis=-1, keepdims=True)
    return (
        rows_float * lax.rsqrt(mean_square + norm_epsilon) * norm_gain.astype(jnp.float32)
    ).astype(jnp.bfloat16)


def visible_pairs(segment, key_count):
    row_index = jnp.arange(segment.shape[0], dtype=jnp.int32)
    key_index = jnp.arange(key_count, dtype=jnp.int32)
    same_segment = (segment[:, None] == segment[None, :]) & (segment[:, None] >= 0)
    causal = key_index[None, :] <= row_index[:, None]
    return same_segment & causal | (key_index[None, :] == row_index[:, None])


def body(hidden_in, norm_gain, w_query, w_key, w_value, w_out, segment):
    pack_rows = segment.shape[0]
    query_cols = w_query.shape[1]
    kv_cols = w_key.shape[1]
    query_heads = query_cols // HEAD
    kv_heads = kv_cols // HEAD
    group_size = query_heads // kv_heads
    score_scale = HEAD ** (-0.5)
    rows_float = hidden_in.astype(jnp.float32)
    normed = rms_normed(rows_float, norm_gain)
    gathered = lax.all_gather(normed, "tensor", axis=0, tiled=True)
    packed = jnp.concatenate((w_query, w_key, w_value, w_out.T), axis=1)
    packed_full = lax.all_gather(packed, "dp", axis=0, tiled=True)
    joined = packed_full[:, : query_cols + 2 * kv_cols]
    out_full_t = packed_full[:, query_cols + 2 * kv_cols :]
    projected = jnp.dot(gathered, joined, preferred_element_type=jnp.float32)
    position = positions_of(segment)
    query_rows = rotate(
        projected[:, :query_cols].reshape(pack_rows, query_heads, HEAD), position
    ).astype(jnp.bfloat16)
    key_rows = rotate(
        projected[:, query_cols : query_cols + kv_cols].reshape(pack_rows, kv_heads, HEAD), position
    ).astype(jnp.bfloat16)
    value_rows = (
        projected[:, query_cols + kv_cols :].astype(jnp.bfloat16).reshape(pack_rows, kv_heads, HEAD)
    )
    cache_rows = jnp.concatenate([key_rows, value_rows], axis=-1)
    grouped_query = query_rows.reshape(pack_rows, kv_heads, group_size, HEAD)
    scores = (
        jnp.einsum("skgh,tkh->kgst", grouped_query, key_rows, preferred_element_type=jnp.float32)
        * score_scale
    )
    allowed = visible_pairs(segment, pack_rows)
    scores = jnp.where(allowed, scores, -1e30)
    row_max = jnp.max(scores, axis=-1, keepdims=True)
    weight = jnp.exp(scores - row_max)
    weight_sum = jnp.sum(weight, axis=-1)
    mixed_rows = (
        jnp.einsum(
            "kgst,tkh->kgsh",
            weight.astype(jnp.bfloat16),
            value_rows,
            preferred_element_type=jnp.float32,
        )
        / weight_sum[..., None]
    )
    attended = (
        jnp.transpose(mixed_rows, (2, 0, 1, 3)).astype(jnp.bfloat16).reshape(pack_rows, query_cols)
    )
    out_rows = lax.dot_general(
        attended, out_full_t, (((1,), (1,)), ((), ())), preferred_element_type=jnp.float32
    )
    summed = lax.psum_scatter(
        out_rows.astype(jnp.bfloat16),
        "tensor",
        scatter_dimension=0,
        tiled=True,
    ).astype(jnp.float32)
    hidden_out = (summed + rows_float).astype(jnp.bfloat16)
    return (hidden_out, cache_rows)


def solution(mesh):
    return jax.shard_map(
        body,
        mesh=mesh,
        in_specs=(
            P(("dp", "tensor"), None),
            P(),
            P("dp", "tensor"),
            P("dp", "tensor"),
            P("dp", "tensor"),
            P("tensor", "dp"),
            P("dp"),
        ),
        out_specs=(P(("dp", "tensor"), None), P("dp", "tensor", None)),
        check_vma=False,
    )
```

```python
import jax
import jax.numpy as jnp
from jax import lax
from jax.sharding import PartitionSpec as P

HEAD = 128


rope_theta = 500000.0
norm_epsilon = 1e-05


def inverse_frequency(head_width):
    exponent = jnp.arange(0, head_width, 2).astype(jnp.float32) / head_width
    base_freq = rope_theta ** (-exponent)
    wavelength = 2.0 * jnp.pi / base_freq
    smooth = (8192.0 / wavelength - 1.0) / 3.0
    blended = (1.0 - smooth) * base_freq / 8.0 + smooth * base_freq
    return jnp.where(
        wavelength < 2048.0, base_freq, jnp.where(wavelength > 8192.0, base_freq / 8.0, blended)
    )


def positions_of(segment):
    row_index = jnp.arange(segment.shape[0], dtype=jnp.int32)
    changed = jnp.concatenate([jnp.ones((1,), dtype=bool), segment[1:] != segment[:-1]])
    begins = lax.cummax(jnp.where(changed, row_index, 0), axis=0)
    return row_index - begins


def rotate(vectors, position):
    head_width = vectors.shape[-1]
    half_width = head_width // 2
    angles = position.astype(jnp.float32)[:, None] * inverse_frequency(head_width)[None, :]
    cosine = jnp.concatenate([jnp.cos(angles), jnp.cos(angles)], axis=-1)[:, None, :]
    sine_table = jnp.concatenate([jnp.sin(angles), jnp.sin(angles)], axis=-1)[:, None, :]
    turned = jnp.concatenate([-vectors[..., half_width:], vectors[..., :half_width]], axis=-1)
    return vectors * cosine + turned * sine_table


def rms_normed(rows_float, norm_gain):
    mean_square = jnp.mean(rows_float * rows_float, axis=-1, keepdims=True)
    return (
        rows_float * lax.rsqrt(mean_square + norm_epsilon) * norm_gain.astype(jnp.float32)
    ).astype(jnp.bfloat16)


def visible_pairs(segment, key_count):
    row_index = jnp.arange(segment.shape[0], dtype=jnp.int32)
    key_index = jnp.arange(key_count, dtype=jnp.int32)
    same_segment = (segment[:, None] == segment[None, :]) & (segment[:, None] >= 0)
    causal = key_index[None, :] <= row_index[:, None]
    return same_segment & causal | (key_index[None, :] == row_index[:, None])


def body(hidden_in, norm_gain, w_query, w_key, w_value, w_out, segment):
    pack_rows = segment.shape[0]
    query_cols = w_query.shape[1]
    kv_cols = w_key.shape[1]
    query_heads = query_cols // HEAD
    kv_heads = kv_cols // HEAD
    group_size = query_heads // kv_heads
    score_scale = HEAD ** (-0.5)
    rows_float = hidden_in.astype(jnp.float32)
    normed = rms_normed(rows_float, norm_gain)
    tensor_size = pack_rows // normed.shape[0]
    gathered = lax.all_to_all(
        jnp.broadcast_to(normed[None], (tensor_size,) + normed.shape), "tensor", 0, 0, tiled=True
    ).reshape(pack_rows, normed.shape[1])
    packed = jnp.concatenate((w_query, w_key, w_value, w_out.T), axis=1)
    packed_full = lax.all_gather(packed, "dp", axis=0, tiled=True)
    joined = packed_full[:, : query_cols + 2 * kv_cols]
    out_full_t = packed_full[:, query_cols + 2 * kv_cols :]
    projected = jnp.dot(gathered, joined, preferred_element_type=jnp.float32)
    position = positions_of(segment)
    query_rows = rotate(
        projected[:, :query_cols].reshape(pack_rows, query_heads, HEAD), position
    ).astype(jnp.bfloat16)
    key_rows = rotate(
        projected[:, query_cols : query_cols + kv_cols].reshape(pack_rows, kv_heads, HEAD), position
    ).astype(jnp.bfloat16)
    value_rows = (
        projected[:, query_cols + kv_cols :].astype(jnp.bfloat16).reshape(pack_rows, kv_heads, HEAD)
    )
    cache_rows = jnp.concatenate([key_rows, value_rows], axis=-1)
    grouped_query = query_rows.reshape(pack_rows, kv_heads, group_size, HEAD)
    scores = (
        jnp.einsum("skgh,tkh->kgst", grouped_query, key_rows, preferred_element_type=jnp.float32)
        * score_scale
    )
    allowed = visible_pairs(segment, pack_rows)
    scores = jnp.where(allowed, scores, -1e30)
    row_max = jnp.max(scores, axis=-1, keepdims=True)
    weight = jnp.exp(scores - row_max)
    weight_sum = jnp.sum(weight, axis=-1)
    mixed_rows = (
        jnp.einsum(
            "kgst,tkh->kgsh",
            weight.astype(jnp.bfloat16),
            value_rows,
            preferred_element_type=jnp.float32,
        )
        / weight_sum[..., None]
    )
    attended = (
        jnp.transpose(mixed_rows, (2, 0, 1, 3)).astype(jnp.bfloat16).reshape(pack_rows, query_cols)
    )
    out_rows = lax.dot_general(
        attended, out_full_t, (((1,), (1,)), ((), ())), preferred_element_type=jnp.float32
    )
    pieces = lax.all_to_all(
        out_rows.astype(jnp.bfloat16).reshape(tensor_size, -1, out_rows.shape[1]), "tensor", 0, 0, tiled=True
    )
    summed = jnp.sum(pieces.astype(jnp.float32), axis=0)
    hidden_out = (summed + rows_float).astype(jnp.bfloat16)
    return (hidden_out, cache_rows)


def solution(mesh):
    return jax.shard_map(
        body,
        mesh=mesh,
        in_specs=(
            P(("dp", "tensor"), None),
            P(),
            P("dp", "tensor"),
            P("dp", "tensor"),
            P("dp", "tensor"),
            P("tensor", "dp"),
            P("dp"),
        ),
        out_specs=(P(("dp", "tensor"), None), P("dp", "tensor", None)),
        check_vma=False,
    )
```

```python
import jax
import jax.numpy as jnp
from jax import lax
from jax.sharding import Mesh, PartitionSpec as P

HEAD = 128


rope_theta = 500000.0
norm_epsilon = 1e-05


def inverse_frequency(head_width):
    exponent = jnp.arange(0, head_width, 2).astype(jnp.float32) / head_width
    base_freq = rope_theta ** (-exponent)
    wavelength = 2.0 * jnp.pi / base_freq
    smooth = (8192.0 / wavelength - 1.0) / 3.0
    blended = (1.0 - smooth) * base_freq / 8.0 + smooth * base_freq
    return jnp.where(
        wavelength < 2048.0, base_freq, jnp.where(wavelength > 8192.0, base_freq / 8.0, blended)
    )


def positions_of(segment):
    row_index = jnp.arange(segment.shape[0], dtype=jnp.int32)
    changed = jnp.concatenate([jnp.ones((1,), dtype=bool), segment[1:] != segment[:-1]])
    begins = lax.cummax(jnp.where(changed, row_index, 0), axis=0)
    return row_index - begins


def rotate(vectors, position):
    head_width = vectors.shape[-1]
    half_width = head_width // 2
    angles = position.astype(jnp.float32)[:, None] * inverse_frequency(head_width)[None, :]
    cosine = jnp.concatenate([jnp.cos(angles), jnp.cos(angles)], axis=-1)[:, None, :]
    sine_table = jnp.concatenate([jnp.sin(angles), jnp.sin(angles)], axis=-1)[:, None, :]
    turned = jnp.concatenate([-vectors[..., half_width:], vectors[..., :half_width]], axis=-1)
    return vectors * cosine + turned * sine_table


def rms_normed(rows_float, norm_gain):
    mean_square = jnp.mean(rows_float * rows_float, axis=-1, keepdims=True)
    return (
        rows_float * lax.rsqrt(mean_square + norm_epsilon) * norm_gain.astype(jnp.float32)
    ).astype(jnp.bfloat16)


def visible_pairs(segment, key_count):
    row_index = jnp.arange(segment.shape[0], dtype=jnp.int32)
    key_index = jnp.arange(key_count, dtype=jnp.int32)
    same_segment = (segment[:, None] == segment[None, :]) & (segment[:, None] >= 0)
    causal = key_index[None, :] <= row_index[:, None]
    return same_segment & causal | (key_index[None, :] == row_index[:, None])


def body(hidden_in, norm_gain, w_query, w_key, w_value, w_out, segment):
    pack_rows = segment.shape[0]
    query_cols = w_query.shape[1]
    kv_cols = w_key.shape[1]
    query_heads = query_cols // HEAD
    kv_heads = kv_cols // HEAD
    group_size = query_heads // kv_heads
    score_scale = HEAD ** (-0.5)
    packed_rows = w_query.shape[0]
    rows_float = hidden_in.astype(jnp.float32)
    normed = rms_normed(rows_float, norm_gain)
    tensor_size = pack_rows // normed.shape[0]
    first_core = lax.axis_index("c") == 0
    split_d = normed.reshape(normed.shape[0], -1, 2, 2, packed_rows)
    by_core = jnp.transpose(split_d, (0, 3, 1, 2, 4))
    by_core = jnp.where(first_core, by_core, by_core[:, ::-1])
    normed = by_core.reshape(normed.shape)
    gathered = lax.all_to_all(
        jnp.broadcast_to(normed[None], (tensor_size,) + normed.shape), "tensor", 0, 0, tiled=True
    ).reshape(pack_rows, normed.shape[1])
    packed = jnp.concatenate((w_query, w_key, w_value, w_out.T), axis=1)
    pair = lax.ppermute(packed, "xl", [(0, 1), (1, 0)])
    first_xl = lax.axis_index("xl") == 0
    chip_pair = jnp.where(
        first_xl, jnp.concatenate((packed, pair)), jnp.concatenate((pair, packed))
    )
    core_half = lax.all_gather(chip_pair, "z", axis=0, tiled=True)
    other_half = lax.ppermute(core_half, "c", [(0, 1), (1, 0)])
    packed_full = jnp.concatenate((core_half, other_half))
    joined = packed_full[:, : query_cols + 2 * kv_cols]
    out_full_t = packed_full[:, query_cols + 2 * kv_cols :]
    projected = jnp.dot(gathered, joined, preferred_element_type=jnp.float32)
    position = positions_of(segment)
    query_rows = rotate(
        projected[:, :query_cols].reshape(pack_rows, query_heads, HEAD), position
    ).astype(jnp.bfloat16)
    key_rows = rotate(
        projected[:, query_cols : query_cols + kv_cols].reshape(pack_rows, kv_heads, HEAD), position
    ).astype(jnp.bfloat16)
    value_rows = (
        projected[:, query_cols + kv_cols :].astype(jnp.bfloat16).reshape(pack_rows, kv_heads, HEAD)
    )
    cache_rows = jnp.concatenate([key_rows, value_rows], axis=-1)
    grouped_query = query_rows.reshape(pack_rows, kv_heads, group_size, HEAD)
    scores = (
        jnp.einsum("skgh,tkh->kgst", grouped_query, key_rows, preferred_element_type=jnp.float32)
        * score_scale
    )
    allowed = visible_pairs(segment, pack_rows)
    scores = jnp.where(allowed, scores, -1e30)
    row_max = jnp.max(scores, axis=-1, keepdims=True)
    weight = jnp.exp(scores - row_max)
    weight_sum = jnp.sum(weight, axis=-1)
    mixed_rows = (
        jnp.einsum(
            "kgst,tkh->kgsh",
            weight.astype(jnp.bfloat16),
            value_rows,
            preferred_element_type=jnp.float32,
        )
        / weight_sum[..., None]
    )
    attended = (
        jnp.transpose(mixed_rows, (2, 0, 1, 3)).astype(jnp.bfloat16).reshape(pack_rows, query_cols)
    )
    out_rows = lax.dot_general(
        attended, out_full_t, (((1,), (1,)), ((), ())), preferred_element_type=jnp.float32
    )
    pieces = lax.all_to_all(
        out_rows.astype(jnp.bfloat16).reshape(tensor_size, -1, out_rows.shape[1]), "tensor", 0, 0, tiled=True
    )
    summed = jnp.sum(pieces.astype(jnp.float32), axis=0)
    split_s = summed.reshape(summed.shape[0], 2, -1, 2, packed_rows)
    split_s = jnp.where(first_core, split_s, split_s[:, ::-1])
    summed = jnp.transpose(split_s, (0, 2, 3, 1, 4)).reshape(summed.shape)
    hidden_out = (summed + rows_float).astype(jnp.bfloat16)
    return (hidden_out, cache_rows)


def solution(mesh):
    dp_size = mesh.shape["dp"]
    chip_mesh = Mesh(
        mesh.devices.reshape(dp_size // 4, 2, 2, mesh.shape["tensor"]), ("z", "xl", "c", "tensor")
    )
    dp = ("z", "xl", "c")
    return jax.shard_map(
        body,
        mesh=chip_mesh,
        in_specs=(
            P((*dp, "tensor"), None),
            P(),
            P(dp, "tensor"),
            P(dp, "tensor"),
            P(dp, "tensor"),
            P("tensor", dp),
            P(dp),
        ),
        out_specs=(P((*dp, "tensor"), None), P(dp, "tensor", None)),
        check_vma=False,
    )
```

```python
import jax
import jax.numpy as jnp
from jax import lax
from jax.sharding import Mesh, PartitionSpec as P

HEAD = 128


rope_theta = 500000.0
norm_epsilon = 1e-05


def inverse_frequency(head_width):
    exponent = jnp.arange(0, head_width, 2).astype(jnp.float32) / head_width
    base_freq = rope_theta ** (-exponent)
    wavelength = 2.0 * jnp.pi / base_freq
    smooth = (8192.0 / wavelength - 1.0) / 3.0
    blended = (1.0 - smooth) * base_freq / 8.0 + smooth * base_freq
    return jnp.where(
        wavelength < 2048.0, base_freq, jnp.where(wavelength > 8192.0, base_freq / 8.0, blended)
    )


def positions_of(segment):
    row_index = jnp.arange(segment.shape[0], dtype=jnp.int32)
    changed = jnp.concatenate([jnp.ones((1,), dtype=bool), segment[1:] != segment[:-1]])
    begins = lax.cummax(jnp.where(changed, row_index, 0), axis=0)
    return row_index - begins


def rotate(vectors, position):
    head_width = vectors.shape[-1]
    half_width = head_width // 2
    angles = position.astype(jnp.float32)[:, None] * inverse_frequency(head_width)[None, :]
    cosine = jnp.concatenate([jnp.cos(angles), jnp.cos(angles)], axis=-1)[:, None, :]
    sine_table = jnp.concatenate([jnp.sin(angles), jnp.sin(angles)], axis=-1)[:, None, :]
    turned = jnp.concatenate([-vectors[..., half_width:], vectors[..., :half_width]], axis=-1)
    return vectors * cosine + turned * sine_table


def rms_normed(rows_float, norm_gain):
    mean_square = jnp.mean(rows_float * rows_float, axis=-1, keepdims=True)
    return (
        rows_float * lax.rsqrt(mean_square + norm_epsilon) * norm_gain.astype(jnp.float32)
    ).astype(jnp.bfloat16)


def visible_pairs(segment, key_count):
    row_index = jnp.arange(segment.shape[0], dtype=jnp.int32)
    key_index = jnp.arange(key_count, dtype=jnp.int32)
    same_segment = (segment[:, None] == segment[None, :]) & (segment[:, None] >= 0)
    causal = key_index[None, :] <= row_index[:, None]
    return same_segment & causal | (key_index[None, :] == row_index[:, None])


def layer(hidden_in, norm_gain, w_query, w_key, w_value, w_out, segment):
    pack_rows = segment.shape[0]
    query_cols = w_query.shape[1]
    kv_cols = w_key.shape[1]
    query_heads = query_cols // HEAD
    kv_heads = kv_cols // HEAD
    group_size = query_heads // kv_heads
    score_scale = HEAD ** (-0.5)
    packed_rows = w_query.shape[0]
    rows_float = hidden_in.astype(jnp.float32)
    normed = rms_normed(rows_float, norm_gain)
    tensor_size = pack_rows // normed.shape[0]
    first_core = lax.axis_index("c") == 0
    split_d = normed.reshape(normed.shape[0], -1, 2, 2, packed_rows)
    by_core = jnp.transpose(split_d, (0, 3, 1, 2, 4))
    by_core = jnp.where(first_core, by_core, by_core[:, ::-1])
    normed = by_core.reshape(normed.shape)
    gathered = lax.all_to_all(
        jnp.broadcast_to(normed[None], (tensor_size,) + normed.shape), "tensor", 0, 0, tiled=True
    ).reshape(pack_rows, normed.shape[1])
    packed = jnp.concatenate((w_query, w_key, w_value, w_out.T), axis=1)
    pair = lax.ppermute(packed, "xl", [(0, 1), (1, 0)])
    first_xl = lax.axis_index("xl") == 0
    chip_pair = jnp.where(
        first_xl, jnp.concatenate((packed, pair)), jnp.concatenate((pair, packed))
    )
    core_half = lax.all_gather(chip_pair, "z", axis=0, tiled=True)
    other_half = lax.ppermute(core_half, "c", [(0, 1), (1, 0)])
    half_rows = core_half.shape[0]
    proj_cols = query_cols + 2 * kv_cols
    projected = jnp.dot(
        gathered[:, :half_rows], core_half[:, :proj_cols], preferred_element_type=jnp.float32
    ) + jnp.dot(
        gathered[:, half_rows:], other_half[:, :proj_cols], preferred_element_type=jnp.float32
    )
    position = positions_of(segment)
    query_rows = rotate(
        projected[:, :query_cols].reshape(pack_rows, query_heads, HEAD), position
    ).astype(jnp.bfloat16)
    key_rows = rotate(
        projected[:, query_cols : query_cols + kv_cols].reshape(pack_rows, kv_heads, HEAD), position
    ).astype(jnp.bfloat16)
    value_rows = (
        projected[:, query_cols + kv_cols :].astype(jnp.bfloat16).reshape(pack_rows, kv_heads, HEAD)
    )
    cache_rows = jnp.concatenate([key_rows, value_rows], axis=-1)
    grouped_query = query_rows.reshape(pack_rows, kv_heads, group_size, HEAD)
    scores = (
        jnp.einsum("skgh,tkh->kgst", grouped_query, key_rows, preferred_element_type=jnp.float32)
        * score_scale
    )
    allowed = visible_pairs(segment, pack_rows)
    scores = jnp.where(allowed, scores, -1e30)
    row_max = jnp.max(scores, axis=-1, keepdims=True)
    weight = jnp.exp(scores - row_max)
    weight_sum = jnp.sum(weight, axis=-1)
    mixed_rows = (
        jnp.einsum(
            "kgst,tkh->kgsh",
            weight.astype(jnp.bfloat16),
            value_rows,
            preferred_element_type=jnp.float32,
        )
        / weight_sum[..., None]
    )
    attended = (
        jnp.transpose(mixed_rows, (2, 0, 1, 3)).astype(jnp.bfloat16).reshape(pack_rows, query_cols)
    )
    out_dims = (((1,), (1,)), ((), ()))
    out_rows = jnp.concatenate(
        (
            lax.dot_general(attended, core_half[:, proj_cols:], out_dims, preferred_element_type=jnp.float32),
            lax.dot_general(attended, other_half[:, proj_cols:], out_dims, preferred_element_type=jnp.float32),
        ),
        axis=1,
    )
    pieces = lax.all_to_all(
        out_rows.astype(jnp.bfloat16).reshape(tensor_size, -1, out_rows.shape[1]), "tensor", 0, 0, tiled=True
    )
    summed = jnp.sum(pieces.astype(jnp.float32), axis=0)
    split_s = summed.reshape(summed.shape[0], 2, -1, 2, packed_rows)
    split_s = jnp.where(first_core, split_s, split_s[:, ::-1])
    summed = jnp.transpose(split_s, (0, 2, 3, 1, 4)).reshape(summed.shape)
    hidden_out = (summed + rows_float).astype(jnp.bfloat16)
    return (hidden_out, cache_rows)


def solution(mesh):
    dp_size = mesh.shape["dp"]
    chip_mesh = Mesh(
        mesh.devices.reshape(dp_size // 4, 2, 2, mesh.shape["tensor"]), ("z", "xl", "c", "tensor")
    )
    dp = ("z", "xl", "c")
    return jax.shard_map(
        layer,
        mesh=chip_mesh,
        in_specs=(
            P((*dp, "tensor"), None),
            P(),
            P(dp, "tensor"),
            P(dp, "tensor"),
            P(dp, "tensor"),
            P("tensor", dp),
            P(dp),
        ),
        out_specs=(P((*dp, "tensor"), None), P(dp, "tensor", None)),
        check_vma=False,
    )
```

```python
import jax
import jax.numpy as jnp
from jax import lax
from jax.sharding import Mesh, PartitionSpec as P

HEAD = 128


rope_theta = 500000.0
norm_epsilon = 1e-05


def inverse_frequency(head_width):
    exponent = jnp.arange(0, head_width, 2).astype(jnp.float32) / head_width
    base_freq = rope_theta ** (-exponent)
    wavelength = 2.0 * jnp.pi / base_freq
    smooth = (8192.0 / wavelength - 1.0) / 3.0
    blended = (1.0 - smooth) * base_freq / 8.0 + smooth * base_freq
    return jnp.where(
        wavelength < 2048.0, base_freq, jnp.where(wavelength > 8192.0, base_freq / 8.0, blended)
    )


def positions_of(segment):
    row_index = jnp.arange(segment.shape[0], dtype=jnp.int32)
    changed = jnp.concatenate([jnp.ones((1,), dtype=bool), segment[1:] != segment[:-1]])
    begins = lax.cummax(jnp.where(changed, row_index, 0), axis=0)
    return row_index - begins


def rotate(vectors, position):
    head_width = vectors.shape[-1]
    half_width = head_width // 2
    angles = position.astype(jnp.float32)[:, None] * inverse_frequency(head_width)[None, :]
    cosine = jnp.concatenate([jnp.cos(angles), jnp.cos(angles)], axis=-1)[:, None, :]
    sine_table = jnp.concatenate([jnp.sin(angles), jnp.sin(angles)], axis=-1)[:, None, :]
    turned = jnp.concatenate([-vectors[..., half_width:], vectors[..., :half_width]], axis=-1)
    return vectors * cosine + turned * sine_table


def rms_normed(rows_float, norm_gain):
    mean_square = jnp.mean(rows_float * rows_float, axis=-1, keepdims=True)
    return (
        rows_float * lax.rsqrt(mean_square + norm_epsilon) * norm_gain.astype(jnp.float32)
    ).astype(jnp.bfloat16)


def visible_pairs(segment, key_count):
    row_index = jnp.arange(segment.shape[0], dtype=jnp.int32)
    key_index = jnp.arange(key_count, dtype=jnp.int32)
    same_segment = (segment[:, None] == segment[None, :]) & (segment[:, None] >= 0)
    causal = key_index[None, :] <= row_index[:, None]
    return same_segment & causal | (key_index[None, :] == row_index[:, None])


def layer(hidden_in, norm_gain, w_query, w_key, w_value, w_out, segment):
    pack_rows = segment.shape[0]
    query_cols = w_query.shape[1]
    kv_cols = w_key.shape[1]
    query_heads = query_cols // HEAD
    kv_heads = kv_cols // HEAD
    group_size = query_heads // kv_heads
    score_scale = HEAD ** (-0.5)
    packed_rows = w_query.shape[0]
    rows_float = hidden_in.astype(jnp.float32)
    normed = rms_normed(rows_float, norm_gain)
    tensor_size = pack_rows // normed.shape[0]
    core = lax.axis_index("c")
    split_d = normed.reshape(normed.shape[0], -1, 2, 2, packed_rows)
    by_core = jnp.transpose(split_d, (0, 3, 1, 2, 4)).reshape(normed.shape[0], 2, -1)
    by_core = lax.dynamic_slice_in_dim(jnp.concatenate((by_core, by_core), axis=1), core, 2, axis=1)
    normed = by_core.reshape(normed.shape)
    gathered = lax.all_to_all(
        jnp.broadcast_to(normed[None], (tensor_size,) + normed.shape), "tensor", 0, 0, tiled=True
    ).reshape(pack_rows, normed.shape[1])
    packed = jnp.concatenate((w_query, w_key, w_value, w_out.T), axis=1)
    pair = lax.ppermute(packed, "xl", [(0, 1), (1, 0)])
    first_xl = lax.axis_index("xl") == 0
    chip_pair = jnp.where(
        first_xl, jnp.concatenate((packed, pair)), jnp.concatenate((pair, packed))
    )
    core_half = lax.all_gather(chip_pair, "z", axis=0, tiled=True)
    other_half = lax.ppermute(core_half, "c", [(0, 1), (1, 0)])
    half_rows = core_half.shape[0]
    proj_cols = query_cols + 2 * kv_cols
    projected = jnp.dot(
        gathered[:, :half_rows], core_half[:, :proj_cols], preferred_element_type=jnp.float32
    ) + jnp.dot(
        gathered[:, half_rows:], other_half[:, :proj_cols], preferred_element_type=jnp.float32
    )
    position = positions_of(segment)
    query_rows = rotate(
        projected[:, :query_cols].reshape(pack_rows, query_heads, HEAD), position
    ).astype(jnp.bfloat16)
    key_rows = rotate(
        projected[:, query_cols : query_cols + kv_cols].reshape(pack_rows, kv_heads, HEAD), position
    ).astype(jnp.bfloat16)
    value_rows = (
        projected[:, query_cols + kv_cols :].astype(jnp.bfloat16).reshape(pack_rows, kv_heads, HEAD)
    )
    cache_rows = jnp.concatenate([key_rows, value_rows], axis=-1)
    grouped_query = query_rows.reshape(pack_rows, kv_heads, group_size, HEAD)
    scores = (
        jnp.einsum("skgh,tkh->kgst", grouped_query, key_rows, preferred_element_type=jnp.float32)
        * score_scale
    )
    allowed = visible_pairs(segment, pack_rows)
    scores = jnp.where(allowed, scores, -1e30)
    row_max = jnp.max(scores, axis=-1, keepdims=True)
    weight = jnp.exp(scores - row_max)
    weight_sum = jnp.sum(weight, axis=-1)
    mixed_rows = (
        jnp.einsum(
            "kgst,tkh->kgsh",
            weight.astype(jnp.bfloat16),
            value_rows,
            preferred_element_type=jnp.float32,
        )
        / weight_sum[..., None]
    )
    attended = (
        jnp.transpose(mixed_rows, (2, 0, 1, 3)).astype(jnp.bfloat16).reshape(pack_rows, query_cols)
    )
    out_dims = (((1,), (1,)), ((), ()))
    out_rows = jnp.concatenate(
        (
            lax.dot_general(attended, core_half[:, proj_cols:], out_dims, preferred_element_type=jnp.float32),
            lax.dot_general(attended, other_half[:, proj_cols:], out_dims, preferred_element_type=jnp.float32),
        ),
        axis=1,
    )
    pieces = lax.all_to_all(
        out_rows.astype(jnp.bfloat16).reshape(tensor_size, -1, out_rows.shape[1]), "tensor", 0, 0, tiled=True
    )
    summed = jnp.sum(pieces.astype(jnp.float32), axis=0)
    split_s = summed.reshape(summed.shape[0], 2, -1)
    split_s = lax.dynamic_slice_in_dim(jnp.concatenate((split_s, split_s), axis=1), core, 2, axis=1)
    split_s = split_s.reshape(summed.shape[0], 2, -1, 2, packed_rows)
    summed = jnp.transpose(split_s, (0, 2, 3, 1, 4)).reshape(summed.shape)
    hidden_out = (summed + rows_float).astype(jnp.bfloat16)
    return (hidden_out, cache_rows)


def solution(mesh):
    dp_size = mesh.shape["dp"]
    chip_mesh = Mesh(
        mesh.devices.reshape(dp_size // 4, 2, 2, mesh.shape["tensor"]), ("z", "xl", "c", "tensor")
    )
    dp = ("z", "xl", "c")
    return jax.shard_map(
        layer,
        mesh=chip_mesh,
        in_specs=(
            P((*dp, "tensor"), None),
            P(),
            P(dp, "tensor"),
            P(dp, "tensor"),
            P(dp, "tensor"),
            P("tensor", dp),
            P(dp),
        ),
        out_specs=(P((*dp, "tensor"), None), P(dp, "tensor", None)),
        check_vma=False,
    )
```

```python
import jax
import jax.numpy as jnp
from jax import lax
from jax.sharding import Mesh, PartitionSpec as P

HEAD = 128


rope_theta = 500000.0
norm_epsilon = 1e-05


def inverse_frequency(head_width):
    exponent = jnp.arange(0, head_width, 2).astype(jnp.float32) / head_width
    base_freq = rope_theta ** (-exponent)
    wavelength = 2.0 * jnp.pi / base_freq
    smooth = (8192.0 / wavelength - 1.0) / 3.0
    blended = (1.0 - smooth) * base_freq / 8.0 + smooth * base_freq
    return jnp.where(
        wavelength < 2048.0, base_freq, jnp.where(wavelength > 8192.0, base_freq / 8.0, blended)
    )


def positions_of(segment):
    row_index = jnp.arange(segment.shape[0], dtype=jnp.int32)
    changed = jnp.concatenate([jnp.ones((1,), dtype=bool), segment[1:] != segment[:-1]])
    begins = lax.cummax(jnp.where(changed, row_index, 0), axis=0)
    return row_index - begins


def rotate(vectors, position):
    head_width = vectors.shape[-1]
    half_width = head_width // 2
    angles = position.astype(jnp.float32)[:, None] * inverse_frequency(head_width)[None, :]
    cosine = jnp.concatenate([jnp.cos(angles), jnp.cos(angles)], axis=-1)[:, None, :]
    sine_table = jnp.concatenate([jnp.sin(angles), jnp.sin(angles)], axis=-1)[:, None, :]
    turned = jnp.concatenate([-vectors[..., half_width:], vectors[..., :half_width]], axis=-1)
    return vectors * cosine + turned * sine_table


def rms_normed(rows_float, norm_gain):
    mean_square = jnp.mean(rows_float * rows_float, axis=-1, keepdims=True)
    return (
        rows_float * lax.rsqrt(mean_square + norm_epsilon) * norm_gain.astype(jnp.float32)
    ).astype(jnp.bfloat16)


def visible_pairs(segment, key_count):
    row_index = jnp.arange(segment.shape[0], dtype=jnp.int32)
    key_index = jnp.arange(key_count, dtype=jnp.int32)
    same_segment = (segment[:, None] == segment[None, :]) & (segment[:, None] >= 0)
    causal = key_index[None, :] <= row_index[:, None]
    return same_segment & causal | (key_index[None, :] == row_index[:, None])


def layer(hidden_in, norm_gain, w_query, w_key, w_value, w_out, segment):
    pack_rows = segment.shape[0]
    query_cols = w_query.shape[1]
    kv_cols = w_key.shape[1]
    query_heads = query_cols // HEAD
    kv_heads = kv_cols // HEAD
    group_size = query_heads // kv_heads
    score_scale = HEAD ** (-0.5)
    packed_rows = w_query.shape[0]
    rows_float = hidden_in.astype(jnp.float32)
    normed = rms_normed(rows_float, norm_gain)
    tensor_size = pack_rows // normed.shape[0]
    core = lax.axis_index("c")
    pair_side = lax.axis_index("xl")
    split_d = normed.reshape(normed.shape[0], -1, 2, 2, packed_rows)
    by_core = jnp.transpose(split_d, (0, 3, 1, 2, 4))
    by_core = lax.dynamic_slice_in_dim(jnp.concatenate((by_core, by_core), axis=1), core, 2, axis=1)
    by_core = lax.dynamic_slice_in_dim(jnp.concatenate((by_core, by_core), axis=3), pair_side, 2, axis=3)
    normed = by_core.reshape(normed.shape)
    gathered = lax.all_to_all(
        jnp.broadcast_to(normed[None], (tensor_size,) + normed.shape), "tensor", 0, 0, tiled=True
    ).reshape(pack_rows, normed.shape[1])
    packed = jnp.concatenate((w_query, w_key, w_value, w_out.T), axis=1)
    pair = lax.ppermute(packed, "xl", [(0, 1), (1, 0)])
    chip_pair = jnp.concatenate((packed, pair))
    core_half = lax.all_gather(chip_pair, "z", axis=0, tiled=True)
    other_half = lax.ppermute(core_half, "c", [(0, 1), (1, 0)])
    half_rows = core_half.shape[0]
    proj_cols = query_cols + 2 * kv_cols
    projected = jnp.dot(
        gathered[:, :half_rows], core_half[:, :proj_cols], preferred_element_type=jnp.float32
    ) + jnp.dot(
        gathered[:, half_rows:], other_half[:, :proj_cols], preferred_element_type=jnp.float32
    )
    position = positions_of(segment)
    query_rows = rotate(
        projected[:, :query_cols].reshape(pack_rows, query_heads, HEAD), position
    ).astype(jnp.bfloat16)
    key_rows = rotate(
        projected[:, query_cols : query_cols + kv_cols].reshape(pack_rows, kv_heads, HEAD), position
    ).astype(jnp.bfloat16)
    value_rows = (
        projected[:, query_cols + kv_cols :].astype(jnp.bfloat16).reshape(pack_rows, kv_heads, HEAD)
    )
    cache_rows = jnp.concatenate([key_rows, value_rows], axis=-1)
    grouped_query = query_rows.reshape(pack_rows, kv_heads, group_size, HEAD)
    scores = (
        jnp.einsum("skgh,tkh->kgst", grouped_query, key_rows, preferred_element_type=jnp.float32)
        * score_scale
    )
    allowed = visible_pairs(segment, pack_rows)
    scores = jnp.where(allowed, scores, -1e30)
    row_max = jnp.max(scores, axis=-1, keepdims=True)
    weight = jnp.exp(scores - row_max)
    weight_sum = jnp.sum(weight, axis=-1)
    mixed_rows = (
        jnp.einsum(
            "kgst,tkh->kgsh",
            weight.astype(jnp.bfloat16),
            value_rows,
            preferred_element_type=jnp.float32,
        )
        / weight_sum[..., None]
    )
    attended = (
        jnp.transpose(mixed_rows, (2, 0, 1, 3)).astype(jnp.bfloat16).reshape(pack_rows, query_cols)
    )
    out_dims = (((1,), (1,)), ((), ()))
    out_rows = jnp.concatenate(
        (
            lax.dot_general(attended, core_half[:, proj_cols:], out_dims, preferred_element_type=jnp.float32),
            lax.dot_general(attended, other_half[:, proj_cols:], out_dims, preferred_element_type=jnp.float32),
        ),
        axis=1,
    )
    pieces = lax.all_to_all(
        out_rows.astype(jnp.bfloat16).reshape(tensor_size, -1, out_rows.shape[1]), "tensor", 0, 0, tiled=True
    )
    summed = jnp.sum(pieces.astype(jnp.float32), axis=0)
    split_s = summed.reshape(summed.shape[0], 2, -1, 2, packed_rows)
    split_s = lax.dynamic_slice_in_dim(jnp.concatenate((split_s, split_s), axis=1), core, 2, axis=1)
    split_s = lax.dynamic_slice_in_dim(jnp.concatenate((split_s, split_s), axis=3), pair_side, 2, axis=3)
    summed = jnp.transpose(split_s, (0, 2, 3, 1, 4)).reshape(summed.shape)
    hidden_out = (summed + rows_float).astype(jnp.bfloat16)
    return (hidden_out, cache_rows)


def solution(mesh):
    dp_size = mesh.shape["dp"]
    chip_mesh = Mesh(
        mesh.devices.reshape(dp_size // 4, 2, 2, mesh.shape["tensor"]), ("z", "xl", "c", "tensor")
    )
    dp = ("z", "xl", "c")
    return jax.shard_map(
        layer,
        mesh=chip_mesh,
        in_specs=(
            P((*dp, "tensor"), None),
            P(),
            P(dp, "tensor"),
            P(dp, "tensor"),
            P(dp, "tensor"),
            P("tensor", dp),
            P(dp),
        ),
        out_specs=(P((*dp, "tensor"), None), P(dp, "tensor", None)),
        check_vma=False,
    )
```

```python
import jax
import jax.numpy as jnp
from jax import lax
from jax.sharding import Mesh, PartitionSpec as P

HEAD = 128


rope_theta = 500000.0
norm_epsilon = 1e-05


def inverse_frequency(head_width):
    exponent = jnp.arange(0, head_width, 2).astype(jnp.float32) / head_width
    base_freq = rope_theta ** (-exponent)
    wavelength = 2.0 * jnp.pi / base_freq
    smooth = (8192.0 / wavelength - 1.0) / 3.0
    blended = (1.0 - smooth) * base_freq / 8.0 + smooth * base_freq
    return jnp.where(
        wavelength < 2048.0, base_freq, jnp.where(wavelength > 8192.0, base_freq / 8.0, blended)
    )


def positions_of(segment):
    row_index = jnp.arange(segment.shape[0], dtype=jnp.int32)
    changed = jnp.concatenate([jnp.ones((1,), dtype=bool), segment[1:] != segment[:-1]])
    begins = lax.cummax(jnp.where(changed, row_index, 0), axis=0)
    return row_index - begins


def rotate(vectors, position):
    head_width = vectors.shape[-1]
    half_width = head_width // 2
    angles = position.astype(jnp.float32)[:, None] * inverse_frequency(head_width)[None, :]
    cosine = jnp.concatenate([jnp.cos(angles), jnp.cos(angles)], axis=-1)[:, None, :]
    sine_table = jnp.concatenate([jnp.sin(angles), jnp.sin(angles)], axis=-1)[:, None, :]
    turned = jnp.concatenate([-vectors[..., half_width:], vectors[..., :half_width]], axis=-1)
    return vectors * cosine + turned * sine_table


def rms_normed(rows_float, norm_gain):
    mean_square = jnp.mean(rows_float * rows_float, axis=-1, keepdims=True)
    return (
        rows_float * lax.rsqrt(mean_square + norm_epsilon) * norm_gain.astype(jnp.float32)
    ).astype(jnp.bfloat16)


def visible_pairs(segment, key_count):
    row_index = jnp.arange(segment.shape[0], dtype=jnp.int32)
    key_index = jnp.arange(key_count, dtype=jnp.int32)
    same_segment = (segment[:, None] == segment[None, :]) & (segment[:, None] >= 0)
    causal = key_index[None, :] <= row_index[:, None]
    return same_segment & causal | (key_index[None, :] == row_index[:, None])


def layer(hidden_in, norm_gain, w_query, w_key, w_value, w_out, segment):
    pack_rows = segment.shape[0]
    query_cols = w_query.shape[1]
    kv_cols = w_key.shape[1]
    query_heads = query_cols // HEAD
    kv_heads = kv_cols // HEAD
    group_size = query_heads // kv_heads
    score_scale = HEAD ** (-0.5)
    packed_rows = w_query.shape[0]
    rows_float = hidden_in.astype(jnp.float32)
    normed = rms_normed(rows_float, norm_gain)
    tensor_size = pack_rows // normed.shape[0]
    core = lax.axis_index("c")
    split_d = normed.reshape(normed.shape[0], -1, 2, 2, packed_rows)
    by_core = jnp.transpose(split_d, (0, 3, 1, 2, 4)).reshape(normed.shape[0], 2, -1)
    by_core = lax.dynamic_slice_in_dim(jnp.concatenate((by_core, by_core), axis=1), core, 2, axis=1)
    normed = by_core.reshape(normed.shape)
    gathered = lax.all_to_all(
        jnp.broadcast_to(normed[None], (tensor_size,) + normed.shape), "tensor", 0, 0, tiled=True
    ).reshape(pack_rows, normed.shape[1])
    packed = jnp.concatenate((w_query, w_key, w_value, w_out.T), axis=1)
    pair = lax.ppermute(packed, "xl", [(0, 1), (1, 0)])
    first_xl = lax.axis_index("xl") == 0
    chip_pair = jnp.where(
        first_xl, jnp.concatenate((packed, pair)), jnp.concatenate((pair, packed))
    )
    core_half = lax.all_gather(chip_pair, "z", axis=0, tiled=True)
    other_half = lax.ppermute(core_half, "c", [(0, 1), (1, 0)])
    half_rows = core_half.shape[0]
    proj_cols = query_cols + 2 * kv_cols
    projected = jnp.dot(
        gathered[:, :half_rows], core_half[:, :proj_cols], preferred_element_type=jnp.float32
    ) + jnp.dot(
        gathered[:, half_rows:], other_half[:, :proj_cols], preferred_element_type=jnp.float32
    )
    position = positions_of(segment)
    query_rows = rotate(
        projected[:, :query_cols].reshape(pack_rows, query_heads, HEAD), position
    ).astype(jnp.bfloat16)
    key_rows = rotate(
        projected[:, query_cols : query_cols + kv_cols].reshape(pack_rows, kv_heads, HEAD), position
    ).astype(jnp.bfloat16)
    value_rows = (
        projected[:, query_cols + kv_cols :].astype(jnp.bfloat16).reshape(pack_rows, kv_heads, HEAD)
    )
    cache_rows = jnp.concatenate([key_rows, value_rows], axis=-1)
    grouped_query = query_rows.reshape(pack_rows, kv_heads, group_size, HEAD)
    scores = (
        jnp.einsum("skgh,tkh->kgst", grouped_query, key_rows, preferred_element_type=jnp.float32)
        * score_scale
    )
    allowed = visible_pairs(segment, pack_rows)
    scores = jnp.where(allowed, scores, -1e30)
    row_max = jnp.max(scores, axis=-1, keepdims=True)
    weight = jnp.exp(scores - row_max)
    weight_sum = jnp.sum(weight, axis=-1)
    mixed_rows = (
        jnp.einsum(
            "kgst,tkh->kgsh",
            weight.astype(jnp.bfloat16),
            value_rows,
            preferred_element_type=jnp.float32,
        )
        / weight_sum[..., None]
    )
    attended = (
        jnp.transpose(mixed_rows, (2, 0, 1, 3)).astype(jnp.bfloat16).reshape(pack_rows, query_cols)
    )
    out_dims = (((1,), (1,)), ((), ()))
    sums = []
    for out_half in (core_half[:, proj_cols:], other_half[:, proj_cols:]):
        part = lax.dot_general(attended, out_half, out_dims, preferred_element_type=jnp.float32)
        got = lax.all_to_all(
            part.astype(jnp.bfloat16).reshape(tensor_size, -1, part.shape[1]), "tensor", 0, 0, tiled=True
        )
        sums.append(jnp.sum(got.astype(jnp.float32), axis=0))
    summed = jnp.concatenate(sums, axis=1)
    split_s = summed.reshape(summed.shape[0], 2, -1)
    split_s = lax.dynamic_slice_in_dim(jnp.concatenate((split_s, split_s), axis=1), core, 2, axis=1)
    split_s = split_s.reshape(summed.shape[0], 2, -1, 2, packed_rows)
    summed = jnp.transpose(split_s, (0, 2, 3, 1, 4)).reshape(summed.shape)
    hidden_out = (summed + rows_float).astype(jnp.bfloat16)
    return (hidden_out, cache_rows)


def solution(mesh):
    dp_size = mesh.shape["dp"]
    chip_mesh = Mesh(
        mesh.devices.reshape(dp_size // 4, 2, 2, mesh.shape["tensor"]), ("z", "xl", "c", "tensor")
    )
    dp = ("z", "xl", "c")
    return jax.shard_map(
        layer,
        mesh=chip_mesh,
        in_specs=(
            P((*dp, "tensor"), None),
            P(),
            P(dp, "tensor"),
            P(dp, "tensor"),
            P(dp, "tensor"),
            P("tensor", dp),
            P(dp),
        ),
        out_specs=(P((*dp, "tensor"), None), P(dp, "tensor", None)),
        check_vma=False,
    )
```

```python
import jax
import jax.numpy as jnp
from jax import lax
from jax.sharding import Mesh, PartitionSpec as P

HEAD = 128


rope_theta = 500000.0
norm_epsilon = 1e-05


def inverse_frequency(head_width):
    exponent = jnp.arange(0, head_width, 2).astype(jnp.float32) / head_width
    base_freq = rope_theta ** (-exponent)
    wavelength = 2.0 * jnp.pi / base_freq
    smooth = (8192.0 / wavelength - 1.0) / 3.0
    blended = (1.0 - smooth) * base_freq / 8.0 + smooth * base_freq
    return jnp.where(
        wavelength < 2048.0, base_freq, jnp.where(wavelength > 8192.0, base_freq / 8.0, blended)
    )


def positions_of(segment):
    row_index = jnp.arange(segment.shape[0], dtype=jnp.int32)
    changed = jnp.concatenate([jnp.ones((1,), dtype=bool), segment[1:] != segment[:-1]])
    begins = lax.cummax(jnp.where(changed, row_index, 0), axis=0)
    return row_index - begins


def rotate(vectors, position):
    head_width = vectors.shape[-1]
    half_width = head_width // 2
    angles = position.astype(jnp.float32)[:, None] * inverse_frequency(head_width)[None, :]
    cosine = jnp.concatenate([jnp.cos(angles), jnp.cos(angles)], axis=-1)[:, None, :]
    sine_table = jnp.concatenate([jnp.sin(angles), jnp.sin(angles)], axis=-1)[:, None, :]
    turned = jnp.concatenate([-vectors[..., half_width:], vectors[..., :half_width]], axis=-1)
    return vectors * cosine + turned * sine_table


def rms_normed(rows_float, norm_gain):
    mean_square = jnp.mean(rows_float * rows_float, axis=-1, keepdims=True)
    return (
        rows_float * lax.rsqrt(mean_square + norm_epsilon) * norm_gain.astype(jnp.float32)
    ).astype(jnp.bfloat16)


def visible_pairs(segment, key_count):
    row_index = jnp.arange(segment.shape[0], dtype=jnp.int32)
    key_index = jnp.arange(key_count, dtype=jnp.int32)
    same_segment = (segment[:, None] == segment[None, :]) & (segment[:, None] >= 0)
    causal = key_index[None, :] <= row_index[:, None]
    return same_segment & causal | (key_index[None, :] == row_index[:, None])


def layer(hidden_in, norm_gain, w_query, w_key, w_value, w_out, segment):
    pack_rows = segment.shape[0]
    query_cols = w_query.shape[1]
    kv_cols = w_key.shape[1]
    query_heads = query_cols // HEAD
    kv_heads = kv_cols // HEAD
    group_size = query_heads // kv_heads
    score_scale = HEAD ** (-0.5)
    packed_rows = w_query.shape[0]
    rows_float = hidden_in.astype(jnp.float32)
    normed = rms_normed(rows_float, norm_gain)
    tensor_size = pack_rows // normed.shape[0]
    core = lax.axis_index("c")
    split_d = normed.reshape(normed.shape[0], -1, 2, 2, packed_rows)
    by_core = jnp.transpose(split_d, (0, 3, 1, 2, 4)).reshape(normed.shape[0], 2, -1)
    by_core = lax.dynamic_slice_in_dim(jnp.concatenate((by_core, by_core), axis=1), core, 2, axis=1)
    normed = by_core.reshape(normed.shape)
    gathered = lax.all_to_all(
        jnp.broadcast_to(normed[None], (tensor_size,) + normed.shape), "tensor", 0, 0, tiled=True
    ).reshape(pack_rows, normed.shape[1])
    packed = jnp.concatenate((w_query, w_key, w_value, w_out.T), axis=1)
    pair = lax.ppermute(packed, "xl", [(0, 1), (1, 0)])
    first_xl = lax.axis_index("xl") == 0
    chip_pair = jnp.where(
        first_xl, jnp.concatenate((packed, pair)), jnp.concatenate((pair, packed))
    )
    core_half = lax.all_gather(chip_pair, "z", axis=0, tiled=True)
    other_half = lax.ppermute(core_half, "c", [(0, 1), (1, 0)])
    half_rows = core_half.shape[0]
    proj_cols = query_cols + 2 * kv_cols
    projected = jnp.dot(
        gathered[:, :half_rows], core_half[:, :proj_cols], preferred_element_type=jnp.float32
    ) + jnp.dot(
        gathered[:, half_rows:], other_half[:, :proj_cols], preferred_element_type=jnp.float32
    )
    position = positions_of(segment)
    query_rows = rotate(
        projected[:, :query_cols].reshape(pack_rows, query_heads, HEAD), position
    ).astype(jnp.bfloat16)
    key_rows = rotate(
        projected[:, query_cols : query_cols + kv_cols].reshape(pack_rows, kv_heads, HEAD), position
    ).astype(jnp.bfloat16)
    value_rows = (
        projected[:, query_cols + kv_cols :].astype(jnp.bfloat16).reshape(pack_rows, kv_heads, HEAD)
    )
    cache_rows = jnp.concatenate([key_rows, value_rows], axis=-1)
    grouped_query = query_rows.reshape(pack_rows, kv_heads, group_size, HEAD)
    scores = (
        jnp.einsum("skgh,tkh->kgst", grouped_query, key_rows, preferred_element_type=jnp.float32)
        * score_scale
    )
    allowed = visible_pairs(segment, pack_rows)
    scores = jnp.where(allowed, scores, -1e30)
    row_max = jnp.max(scores, axis=-1, keepdims=True)
    weight = jnp.exp(scores - row_max)
    weight_sum = jnp.sum(weight, axis=-1)
    mixed_rows = (
        jnp.einsum(
            "kgst,tkh->kgsh",
            weight.astype(jnp.bfloat16),
            value_rows,
            preferred_element_type=jnp.float32,
        )
        / weight_sum[..., None]
    )
    attended = (
        jnp.transpose(mixed_rows, (2, 0, 1, 3)).astype(jnp.bfloat16).reshape(pack_rows, query_cols)
    )
    out_dims = (((1,), (1,)), ((), ()))
    out_rows = jnp.concatenate(
        (
            lax.dot_general(attended, core_half[:, proj_cols:], out_dims, preferred_element_type=jnp.float32),
            lax.dot_general(attended, other_half[:, proj_cols:], out_dims, preferred_element_type=jnp.float32),
        ),
        axis=1,
    )
    pieces = lax.all_to_all(
        out_rows.astype(jnp.bfloat16).reshape(tensor_size, -1, out_rows.shape[1]), "tensor", 0, 0, tiled=True
    )
    summed = jnp.sum(pieces.astype(jnp.float32), axis=0)
    split_r = hidden_in.reshape(hidden_in.shape[0], -1, 2, 2, packed_rows)
    split_r = jnp.transpose(split_r, (0, 3, 1, 2, 4)).reshape(hidden_in.shape[0], 2, -1)
    split_r = lax.dynamic_slice_in_dim(jnp.concatenate((split_r, split_r), axis=1), core, 2, axis=1)
    residual = split_r.reshape(hidden_in.shape).astype(jnp.float32)
    hidden_perm = (summed + residual).astype(jnp.bfloat16)
    split_s = hidden_perm.reshape(hidden_perm.shape[0], 2, -1)
    split_s = lax.dynamic_slice_in_dim(jnp.concatenate((split_s, split_s), axis=1), core, 2, axis=1)
    split_s = split_s.reshape(hidden_perm.shape[0], 2, -1, 2, packed_rows)
    hidden_out = jnp.transpose(split_s, (0, 2, 3, 1, 4)).reshape(hidden_perm.shape)
    return (hidden_out, cache_rows)


def solution(mesh):
    dp_size = mesh.shape["dp"]
    chip_mesh = Mesh(
        mesh.devices.reshape(dp_size // 4, 2, 2, mesh.shape["tensor"]), ("z", "xl", "c", "tensor")
    )
    dp = ("z", "xl", "c")
    return jax.shard_map(
        layer,
        mesh=chip_mesh,
        in_specs=(
            P((*dp, "tensor"), None),
            P(),
            P(dp, "tensor"),
            P(dp, "tensor"),
            P(dp, "tensor"),
            P("tensor", dp),
            P(dp),
        ),
        out_specs=(P((*dp, "tensor"), None), P(dp, "tensor", None)),
        check_vma=False,
    )
```

```python
import jax
import jax.numpy as jnp
from jax import lax
from jax.sharding import Mesh, PartitionSpec as P

HEAD = 128


rope_theta = 500000.0
norm_epsilon = 1e-05


def inverse_frequency(head_width):
    exponent = jnp.arange(0, head_width, 2).astype(jnp.float32) / head_width
    base_freq = rope_theta ** (-exponent)
    wavelength = 2.0 * jnp.pi / base_freq
    smooth = (8192.0 / wavelength - 1.0) / 3.0
    blended = (1.0 - smooth) * base_freq / 8.0 + smooth * base_freq
    return jnp.where(
        wavelength < 2048.0, base_freq, jnp.where(wavelength > 8192.0, base_freq / 8.0, blended)
    )


def positions_of(segment):
    row_index = jnp.arange(segment.shape[0], dtype=jnp.int32)
    changed = jnp.concatenate([jnp.ones((1,), dtype=bool), segment[1:] != segment[:-1]])
    begins = lax.cummax(jnp.where(changed, row_index, 0), axis=0)
    return row_index - begins


def rotate(vectors, position):
    head_width = vectors.shape[-1]
    half_width = head_width // 2
    angles = position.astype(jnp.float32)[:, None] * inverse_frequency(head_width)[None, :]
    cosine = jnp.concatenate([jnp.cos(angles), jnp.cos(angles)], axis=-1)[:, None, :]
    sine_table = jnp.concatenate([jnp.sin(angles), jnp.sin(angles)], axis=-1)[:, None, :]
    turned = jnp.concatenate([-vectors[..., half_width:], vectors[..., :half_width]], axis=-1)
    return vectors * cosine + turned * sine_table


def rms_normed(rows_float, norm_gain):
    mean_square = jnp.mean(rows_float * rows_float, axis=-1, keepdims=True)
    return (
        rows_float * lax.rsqrt(mean_square + norm_epsilon) * norm_gain.astype(jnp.float32)
    ).astype(jnp.bfloat16)


def visible_pairs(segment, key_count):
    row_index = jnp.arange(segment.shape[0], dtype=jnp.int32)
    key_index = jnp.arange(key_count, dtype=jnp.int32)
    same_segment = (segment[:, None] == segment[None, :]) & (segment[:, None] >= 0)
    causal = key_index[None, :] <= row_index[:, None]
    return same_segment & causal | (key_index[None, :] == row_index[:, None])


def layer(hidden_in, norm_gain, w_query, w_key, w_value, w_out, segment):
    pack_rows = segment.shape[0]
    query_cols = w_query.shape[1]
    kv_cols = w_key.shape[1]
    query_heads = query_cols // HEAD
    kv_heads = kv_cols // HEAD
    group_size = query_heads // kv_heads
    score_scale = HEAD ** (-0.5)
    packed_rows = w_query.shape[0]
    rows_float = hidden_in.astype(jnp.float32)
    normed = rms_normed(rows_float, norm_gain)
    tensor_size = pack_rows // normed.shape[0]
    core = lax.axis_index("c")
    split_d = normed.reshape(normed.shape[0], -1, 2, 2, packed_rows)
    by_core = jnp.transpose(split_d, (0, 3, 1, 2, 4)).reshape(normed.shape[0], 2, -1)
    by_core = lax.dynamic_slice_in_dim(jnp.concatenate((by_core, by_core), axis=1), core, 2, axis=1)
    normed = by_core.reshape(normed.shape)
    gathered = lax.all_to_all(
        jnp.broadcast_to(normed[None], (tensor_size,) + normed.shape), "tensor", 0, 0, tiled=True
    ).reshape(pack_rows, normed.shape[1])
    packed = jnp.concatenate((w_query, w_key, w_value, w_out.T), axis=1)
    pair = lax.ppermute(packed, "xl", [(0, 1), (1, 0)])
    first_xl = lax.axis_index("xl") == 0
    chip_pair = jnp.where(
        first_xl, jnp.concatenate((packed, pair)), jnp.concatenate((pair, packed))
    )
    core_half = lax.all_gather(chip_pair, "z", axis=0, tiled=True)
    other_half = lax.ppermute(core_half, "c", [(0, 1), (1, 0)])
    half_rows = core_half.shape[0]
    proj_cols = query_cols + 2 * kv_cols
    own_part = jnp.dot(
        gathered[:, :half_rows], core_half[:, :proj_cols], preferred_element_type=jnp.float32
    )
    own_part = lax.optimization_barrier(own_part)
    projected = own_part + jnp.dot(
        gathered[:, half_rows:], other_half[:, :proj_cols], preferred_element_type=jnp.float32
    )
    position = positions_of(segment)
    query_rows = rotate(
        projected[:, :query_cols].reshape(pack_rows, query_heads, HEAD), position
    ).astype(jnp.bfloat16)
    key_rows = rotate(
        projected[:, query_cols : query_cols + kv_cols].reshape(pack_rows, kv_heads, HEAD), position
    ).astype(jnp.bfloat16)
    value_rows = (
        projected[:, query_cols + kv_cols :].astype(jnp.bfloat16).reshape(pack_rows, kv_heads, HEAD)
    )
    cache_rows = jnp.concatenate([key_rows, value_rows], axis=-1)
    grouped_query = query_rows.reshape(pack_rows, kv_heads, group_size, HEAD)
    scores = (
        jnp.einsum("skgh,tkh->kgst", grouped_query, key_rows, preferred_element_type=jnp.float32)
        * score_scale
    )
    allowed = visible_pairs(segment, pack_rows)
    scores = jnp.where(allowed, scores, -1e30)
    row_max = jnp.max(scores, axis=-1, keepdims=True)
    weight = jnp.exp(scores - row_max)
    weight_sum = jnp.sum(weight, axis=-1)
    mixed_rows = (
        jnp.einsum(
            "kgst,tkh->kgsh",
            weight.astype(jnp.bfloat16),
            value_rows,
            preferred_element_type=jnp.float32,
        )
        / weight_sum[..., None]
    )
    attended = (
        jnp.transpose(mixed_rows, (2, 0, 1, 3)).astype(jnp.bfloat16).reshape(pack_rows, query_cols)
    )
    out_dims = (((1,), (1,)), ((), ()))
    out_rows = jnp.concatenate(
        (
            lax.dot_general(attended, core_half[:, proj_cols:], out_dims, preferred_element_type=jnp.float32),
            lax.dot_general(attended, other_half[:, proj_cols:], out_dims, preferred_element_type=jnp.float32),
        ),
        axis=1,
    )
    pieces = lax.all_to_all(
        out_rows.astype(jnp.bfloat16).reshape(tensor_size, -1, out_rows.shape[1]), "tensor", 0, 0, tiled=True
    )
    summed = jnp.sum(pieces.astype(jnp.float32), axis=0)
    split_s = summed.reshape(summed.shape[0], 2, -1)
    split_s = lax.dynamic_slice_in_dim(jnp.concatenate((split_s, split_s), axis=1), core, 2, axis=1)
    split_s = split_s.reshape(summed.shape[0], 2, -1, 2, packed_rows)
    summed = jnp.transpose(split_s, (0, 2, 3, 1, 4)).reshape(summed.shape)
    hidden_out = (summed + rows_float).astype(jnp.bfloat16)
    return (hidden_out, cache_rows)


def solution(mesh):
    dp_size = mesh.shape["dp"]
    chip_mesh = Mesh(
        mesh.devices.reshape(dp_size // 4, 2, 2, mesh.shape["tensor"]), ("z", "xl", "c", "tensor")
    )
    dp = ("z", "xl", "c")
    return jax.shard_map(
        layer,
        mesh=chip_mesh,
        in_specs=(
            P((*dp, "tensor"), None),
            P(),
            P(dp, "tensor"),
            P(dp, "tensor"),
            P(dp, "tensor"),
            P("tensor", dp),
            P(dp),
        ),
        out_specs=(P((*dp, "tensor"), None), P(dp, "tensor", None)),
        check_vma=False,
    )
```

```python
import jax
import jax.numpy as jnp
from jax import lax
from jax.sharding import Mesh, PartitionSpec as P

HEAD = 128


rope_theta = 500000.0
norm_epsilon = 1e-05


def inverse_frequency(head_width):
    exponent = jnp.arange(0, head_width, 2).astype(jnp.float32) / head_width
    base_freq = rope_theta ** (-exponent)
    wavelength = 2.0 * jnp.pi / base_freq
    smooth = (8192.0 / wavelength - 1.0) / 3.0
    blended = (1.0 - smooth) * base_freq / 8.0 + smooth * base_freq
    return jnp.where(
        wavelength < 2048.0, base_freq, jnp.where(wavelength > 8192.0, base_freq / 8.0, blended)
    )


def positions_of(segment):
    row_index = jnp.arange(segment.shape[0], dtype=jnp.int32)
    changed = jnp.concatenate([jnp.ones((1,), dtype=bool), segment[1:] != segment[:-1]])
    begins = lax.cummax(jnp.where(changed, row_index, 0), axis=0)
    return row_index - begins


def rotate(vectors, position):
    head_width = vectors.shape[-1]
    half_width = head_width // 2
    angles = position.astype(jnp.float32)[:, None] * inverse_frequency(head_width)[None, :]
    cosine = jnp.concatenate([jnp.cos(angles), jnp.cos(angles)], axis=-1)[:, None, :]
    sine_table = jnp.concatenate([jnp.sin(angles), jnp.sin(angles)], axis=-1)[:, None, :]
    turned = jnp.concatenate([-vectors[..., half_width:], vectors[..., :half_width]], axis=-1)
    return vectors * cosine + turned * sine_table


def rms_normed(rows_float, norm_gain):
    mean_square = jnp.mean(rows_float * rows_float, axis=-1, keepdims=True)
    return (
        rows_float * lax.rsqrt(mean_square + norm_epsilon) * norm_gain.astype(jnp.float32)
    ).astype(jnp.bfloat16)


def visible_pairs(segment, key_count):
    row_index = jnp.arange(segment.shape[0], dtype=jnp.int32)
    key_index = jnp.arange(key_count, dtype=jnp.int32)
    same_segment = (segment[:, None] == segment[None, :]) & (segment[:, None] >= 0)
    causal = key_index[None, :] <= row_index[:, None]
    return same_segment & causal | (key_index[None, :] == row_index[:, None])


def layer(hidden_in, norm_gain, w_query, w_key, w_value, w_out, segment):
    pack_rows = segment.shape[0]
    query_cols = w_query.shape[1]
    kv_cols = w_key.shape[1]
    query_heads = query_cols // HEAD
    kv_heads = kv_cols // HEAD
    group_size = query_heads // kv_heads
    score_scale = HEAD ** (-0.5)
    packed_rows = w_query.shape[0]
    rows_float = hidden_in.astype(jnp.float32)
    normed = rms_normed(rows_float, norm_gain)
    tensor_size = pack_rows // normed.shape[0]
    core = lax.axis_index("c")
    split_d = normed.reshape(normed.shape[0], -1, 2, 2, packed_rows)
    by_core = jnp.transpose(split_d, (0, 3, 1, 2, 4)).reshape(normed.shape[0], 2, -1)
    by_core = lax.dynamic_slice_in_dim(jnp.concatenate((by_core, by_core), axis=1), core, 2, axis=1)
    normed = by_core.reshape(normed.shape)
    gathered = lax.all_to_all(
        jnp.broadcast_to(normed[None], (tensor_size,) + normed.shape), "tensor", 0, 0, tiled=True
    ).reshape(pack_rows, normed.shape[1])
    packed = jnp.concatenate((w_query, w_key, w_value, w_out.T), axis=1)
    pair = lax.ppermute(packed, "xl", [(0, 1), (1, 0)])
    first_xl = lax.axis_index("xl") == 0
    chip_pair = jnp.where(
        first_xl, jnp.concatenate((packed, pair)), jnp.concatenate((pair, packed))
    )
    core_half = lax.all_gather(chip_pair, "z", axis=0, tiled=True)
    other_half = lax.ppermute(core_half, "c", [(0, 1), (1, 0)])
    half_rows = core_half.shape[0]
    proj_cols = query_cols + 2 * kv_cols
    own_part = jnp.dot(
        gathered[:, :half_rows], core_half[:, :proj_cols], preferred_element_type=jnp.float32
    )
    own_part = lax.optimization_barrier(own_part)
    projected = own_part + jnp.dot(
        gathered[:, half_rows:], other_half[:, :proj_cols], preferred_element_type=jnp.float32
    )
    position = positions_of(segment)
    query_rows = rotate(
        projected[:, :query_cols].reshape(pack_rows, query_heads, HEAD), position
    ).astype(jnp.bfloat16)
    key_rows = rotate(
        projected[:, query_cols : query_cols + kv_cols].reshape(pack_rows, kv_heads, HEAD), position
    ).astype(jnp.bfloat16)
    value_rows = (
        projected[:, query_cols + kv_cols :].astype(jnp.bfloat16).reshape(pack_rows, kv_heads, HEAD)
    )
    cache_rows = jnp.concatenate([key_rows, value_rows], axis=-1)
    grouped_query = query_rows.reshape(pack_rows, kv_heads, group_size, HEAD)
    scores = (
        jnp.einsum("skgh,tkh->kgst", grouped_query, key_rows, preferred_element_type=jnp.float32)
        * score_scale
    )
    allowed = visible_pairs(segment, pack_rows)
    scores = jnp.where(allowed, scores, -1e30)
    row_max = jnp.max(scores, axis=-1, keepdims=True)
    weight = jnp.exp(scores - row_max)
    weight_sum = jnp.sum(weight, axis=-1)
    mixed_rows = (
        jnp.einsum(
            "kgst,tkh->kgsh",
            weight.astype(jnp.bfloat16),
            value_rows,
            preferred_element_type=jnp.float32,
        )
        / weight_sum[..., None]
    )
    attended = (
        jnp.transpose(mixed_rows, (2, 0, 1, 3)).astype(jnp.bfloat16).reshape(pack_rows, query_cols)
    )
    out_dims = (((1,), (1,)), ((), ()))
    out_rows = jnp.concatenate(
        (
            lax.dot_general(attended, core_half[:, proj_cols:], out_dims, preferred_element_type=jnp.float32),
            lax.dot_general(attended, other_half[:, proj_cols:], out_dims, preferred_element_type=jnp.float32),
        ),
        axis=1,
    )
    pieces = lax.all_to_all(
        out_rows.astype(jnp.bfloat16).reshape(tensor_size, -1, out_rows.shape[1]), "tensor", 0, 0, tiled=True
    )
    summed = jnp.sum(pieces.astype(jnp.float32), axis=0)
    split_r = hidden_in.reshape(hidden_in.shape[0], -1, 2, 2, packed_rows)
    split_r = jnp.transpose(split_r, (0, 3, 1, 2, 4)).reshape(hidden_in.shape[0], 2, -1)
    split_r = lax.dynamic_slice_in_dim(jnp.concatenate((split_r, split_r), axis=1), core, 2, axis=1)
    residual = split_r.reshape(hidden_in.shape).astype(jnp.float32)
    hidden_perm = (summed + residual).astype(jnp.bfloat16)
    split_s = hidden_perm.reshape(hidden_perm.shape[0], 2, -1)
    split_s = lax.dynamic_slice_in_dim(jnp.concatenate((split_s, split_s), axis=1), core, 2, axis=1)
    split_s = split_s.reshape(hidden_perm.shape[0], 2, -1, 2, packed_rows)
    hidden_out = jnp.transpose(split_s, (0, 2, 3, 1, 4)).reshape(hidden_perm.shape)
    return (hidden_out, cache_rows)


def solution(mesh):
    dp_size = mesh.shape["dp"]
    chip_mesh = Mesh(
        mesh.devices.reshape(dp_size // 4, 2, 2, mesh.shape["tensor"]), ("z", "xl", "c", "tensor")
    )
    dp = ("z", "xl", "c")
    return jax.shard_map(
        layer,
        mesh=chip_mesh,
        in_specs=(
            P((*dp, "tensor"), None),
            P(),
            P(dp, "tensor"),
            P(dp, "tensor"),
            P(dp, "tensor"),
            P("tensor", dp),
            P(dp),
        ),
        out_specs=(P((*dp, "tensor"), None), P(dp, "tensor", None)),
        check_vma=False,
    )
```

```python
import jax
import jax.numpy as jnp
from jax import lax
from jax.sharding import Mesh, PartitionSpec as P

HEAD = 128


rope_theta = 500000.0
norm_epsilon = 1e-05


def inverse_frequency(head_width):
    exponent = jnp.arange(0, head_width, 2).astype(jnp.float32) / head_width
    base_freq = rope_theta ** (-exponent)
    wavelength = 2.0 * jnp.pi / base_freq
    smooth = (8192.0 / wavelength - 1.0) / 3.0
    blended = (1.0 - smooth) * base_freq / 8.0 + smooth * base_freq
    return jnp.where(
        wavelength < 2048.0, base_freq, jnp.where(wavelength > 8192.0, base_freq / 8.0, blended)
    )


def positions_of(segment):
    row_index = jnp.arange(segment.shape[0], dtype=jnp.int32)
    changed = jnp.concatenate([jnp.ones((1,), dtype=bool), segment[1:] != segment[:-1]])
    begins = lax.cummax(jnp.where(changed, row_index, 0), axis=0)
    return row_index - begins


def rotate(vectors, position):
    head_width = vectors.shape[-1]
    half_width = head_width // 2
    angles = position.astype(jnp.float32)[:, None] * inverse_frequency(head_width)[None, :]
    cosine = jnp.concatenate([jnp.cos(angles), jnp.cos(angles)], axis=-1)[:, None, :]
    sine_table = jnp.concatenate([jnp.sin(angles), jnp.sin(angles)], axis=-1)[:, None, :]
    turned = jnp.concatenate([-vectors[..., half_width:], vectors[..., :half_width]], axis=-1)
    return vectors * cosine + turned * sine_table


def rms_normed(rows_float, norm_gain):
    mean_square = jnp.mean(rows_float * rows_float, axis=-1, keepdims=True)
    return (
        rows_float * lax.rsqrt(mean_square + norm_epsilon) * norm_gain.astype(jnp.float32)
    ).astype(jnp.bfloat16)


def visible_pairs(segment, key_count):
    row_index = jnp.arange(segment.shape[0], dtype=jnp.int32)
    key_index = jnp.arange(key_count, dtype=jnp.int32)
    same_segment = (segment[:, None] == segment[None, :]) & (segment[:, None] >= 0)
    causal = key_index[None, :] <= row_index[:, None]
    return same_segment & causal | (key_index[None, :] == row_index[:, None])


def layer(hidden_in, norm_gain, w_query, w_key, w_value, w_out, segment):
    pack_rows = segment.shape[0]
    query_cols = w_query.shape[1]
    kv_cols = w_key.shape[1]
    query_heads = query_cols // HEAD
    kv_heads = kv_cols // HEAD
    group_size = query_heads // kv_heads
    score_scale = HEAD ** (-0.5)
    packed_rows = w_query.shape[0]
    rows_float = hidden_in.astype(jnp.float32)
    normed = rms_normed(rows_float, norm_gain)
    tensor_size = pack_rows // normed.shape[0]
    core = lax.axis_index("c")
    split_d = normed.reshape(normed.shape[0], -1, 2, 2, packed_rows)
    by_core = jnp.transpose(split_d, (0, 3, 1, 2, 4)).reshape(normed.shape[0], 2, -1)
    by_core = lax.dynamic_slice_in_dim(jnp.concatenate((by_core, by_core), axis=1), core, 2, axis=1)
    normed = by_core.reshape(normed.shape)
    gathered = lax.all_to_all(
        jnp.broadcast_to(normed[None], (tensor_size,) + normed.shape), "tensor", 0, 0, tiled=True
    ).reshape(pack_rows, normed.shape[1])
    packed = jnp.concatenate((w_query, w_key, w_value, w_out.T), axis=1)
    pair = lax.ppermute(packed, "xl", [(0, 1), (1, 0)])
    first_xl = lax.axis_index("xl") == 0
    chip_pair = jnp.where(
        first_xl, jnp.concatenate((packed, pair)), jnp.concatenate((pair, packed))
    )
    core_half = lax.all_gather(chip_pair, "z", axis=0, tiled=True)
    proj_cols = query_cols + 2 * kv_cols
    other_proj = lax.ppermute(core_half[:, :proj_cols], "c", [(0, 1), (1, 0)])
    other_out = lax.ppermute(core_half[:, proj_cols:], "c", [(0, 1), (1, 0)])
    half_rows = core_half.shape[0]
    own_part = jnp.dot(
        gathered[:, :half_rows], core_half[:, :proj_cols], preferred_element_type=jnp.float32
    )
    own_part = lax.optimization_barrier(own_part)
    projected = own_part + jnp.dot(
        gathered[:, half_rows:], other_proj, preferred_element_type=jnp.float32
    )
    position = positions_of(segment)
    query_rows = rotate(
        projected[:, :query_cols].reshape(pack_rows, query_heads, HEAD), position
    ).astype(jnp.bfloat16)
    key_rows = rotate(
        projected[:, query_cols : query_cols + kv_cols].reshape(pack_rows, kv_heads, HEAD), position
    ).astype(jnp.bfloat16)
    value_rows = (
        projected[:, query_cols + kv_cols :].astype(jnp.bfloat16).reshape(pack_rows, kv_heads, HEAD)
    )
    cache_rows = jnp.concatenate([key_rows, value_rows], axis=-1)
    grouped_query = query_rows.reshape(pack_rows, kv_heads, group_size, HEAD)
    scores = (
        jnp.einsum("skgh,tkh->kgst", grouped_query, key_rows, preferred_element_type=jnp.float32)
        * score_scale
    )
    allowed = visible_pairs(segment, pack_rows)
    scores = jnp.where(allowed, scores, -1e30)
    row_max = jnp.max(scores, axis=-1, keepdims=True)
    weight = jnp.exp(scores - row_max)
    weight_sum = jnp.sum(weight, axis=-1)
    mixed_rows = (
        jnp.einsum(
            "kgst,tkh->kgsh",
            weight.astype(jnp.bfloat16),
            value_rows,
            preferred_element_type=jnp.float32,
        )
        / weight_sum[..., None]
    )
    attended = (
        jnp.transpose(mixed_rows, (2, 0, 1, 3)).astype(jnp.bfloat16).reshape(pack_rows, query_cols)
    )
    out_dims = (((1,), (1,)), ((), ()))
    out_rows = jnp.concatenate(
        (
            lax.dot_general(attended, core_half[:, proj_cols:], out_dims, preferred_element_type=jnp.float32),
            lax.dot_general(attended, other_out, out_dims, preferred_element_type=jnp.float32),
        ),
        axis=1,
    )
    pieces = lax.all_to_all(
        out_rows.astype(jnp.bfloat16).reshape(tensor_size, -1, out_rows.shape[1]), "tensor", 0, 0, tiled=True
    )
    summed = jnp.sum(pieces.astype(jnp.float32), axis=0)
    split_s = summed.reshape(summed.shape[0], 2, -1)
    split_s = lax.dynamic_slice_in_dim(jnp.concatenate((split_s, split_s), axis=1), core, 2, axis=1)
    split_s = split_s.reshape(summed.shape[0], 2, -1, 2, packed_rows)
    summed = jnp.transpose(split_s, (0, 2, 3, 1, 4)).reshape(summed.shape)
    hidden_out = (summed + rows_float).astype(jnp.bfloat16)
    return (hidden_out, cache_rows)


def solution(mesh):
    dp_size = mesh.shape["dp"]
    chip_mesh = Mesh(
        mesh.devices.reshape(dp_size // 4, 2, 2, mesh.shape["tensor"]), ("z", "xl", "c", "tensor")
    )
    dp = ("z", "xl", "c")
    return jax.shard_map(
        layer,
        mesh=chip_mesh,
        in_specs=(
            P((*dp, "tensor"), None),
            P(),
            P(dp, "tensor"),
            P(dp, "tensor"),
            P(dp, "tensor"),
            P("tensor", dp),
            P(dp),
        ),
        out_specs=(P((*dp, "tensor"), None), P(dp, "tensor", None)),
        check_vma=False,
    )
```

```python
import jax
import jax.numpy as jnp
from jax import lax
from jax.sharding import Mesh, PartitionSpec as P

HEAD = 128


rope_theta = 500000.0
norm_epsilon = 1e-05


def inverse_frequency(head_width):
    exponent = jnp.arange(0, head_width, 2).astype(jnp.float32) / head_width
    base_freq = rope_theta ** (-exponent)
    wavelength = 2.0 * jnp.pi / base_freq
    smooth = (8192.0 / wavelength - 1.0) / 3.0
    blended = (1.0 - smooth) * base_freq / 8.0 + smooth * base_freq
    return jnp.where(
        wavelength < 2048.0, base_freq, jnp.where(wavelength > 8192.0, base_freq / 8.0, blended)
    )


def positions_of(segment):
    row_index = jnp.arange(segment.shape[0], dtype=jnp.int32)
    changed = jnp.concatenate([jnp.ones((1,), dtype=bool), segment[1:] != segment[:-1]])
    begins = lax.cummax(jnp.where(changed, row_index, 0), axis=0)
    return row_index - begins


def rotate(vectors, position):
    head_width = vectors.shape[-1]
    half_width = head_width // 2
    angles = position.astype(jnp.float32)[:, None] * inverse_frequency(head_width)[None, :]
    cosine = jnp.concatenate([jnp.cos(angles), jnp.cos(angles)], axis=-1)[:, None, :]
    sine_table = jnp.concatenate([jnp.sin(angles), jnp.sin(angles)], axis=-1)[:, None, :]
    turned = jnp.concatenate([-vectors[..., half_width:], vectors[..., :half_width]], axis=-1)
    return vectors * cosine + turned * sine_table


def rms_normed(rows_float, norm_gain):
    mean_square = jnp.mean(rows_float * rows_float, axis=-1, keepdims=True)
    return (
        rows_float * lax.rsqrt(mean_square + norm_epsilon) * norm_gain.astype(jnp.float32)
    ).astype(jnp.bfloat16)


def visible_pairs(segment, key_count):
    row_index = jnp.arange(segment.shape[0], dtype=jnp.int32)
    key_index = jnp.arange(key_count, dtype=jnp.int32)
    same_segment = (segment[:, None] == segment[None, :]) & (segment[:, None] >= 0)
    causal = key_index[None, :] <= row_index[:, None]
    return same_segment & causal | (key_index[None, :] == row_index[:, None])


def layer(hidden_in, norm_gain, w_query, w_key, w_value, w_out, segment):
    pack_rows = segment.shape[0]
    query_cols = w_query.shape[1]
    kv_cols = w_key.shape[1]
    query_heads = query_cols // HEAD
    kv_heads = kv_cols // HEAD
    group_size = query_heads // kv_heads
    score_scale = HEAD ** (-0.5)
    packed_rows = w_query.shape[0]
    rows_float = hidden_in.astype(jnp.float32)
    normed = rms_normed(rows_float, norm_gain)
    tensor_size = pack_rows // normed.shape[0]
    core = lax.axis_index("c")
    pair_side = lax.axis_index("xl")
    split_d = normed.reshape(normed.shape[0], -1, 2, 2, packed_rows)
    by_core = jnp.transpose(split_d, (0, 3, 1, 2, 4))
    by_core = lax.dynamic_slice_in_dim(jnp.concatenate((by_core, by_core), axis=1), core, 2, axis=1)
    by_core = lax.dynamic_slice_in_dim(jnp.concatenate((by_core, by_core), axis=3), pair_side, 2, axis=3)
    normed = by_core.reshape(normed.shape)
    gathered = lax.all_to_all(
        jnp.broadcast_to(normed[None], (tensor_size,) + normed.shape), "tensor", 0, 0, tiled=True
    ).reshape(pack_rows, normed.shape[1])
    shards = (w_query, w_key, w_value, w_out.T)
    pairs = tuple(lax.ppermute(w, "xl", [(0, 1), (1, 0)]) for w in shards)
    chip_pair = jnp.concatenate(
        (jnp.concatenate(shards, axis=1), jnp.concatenate(pairs, axis=1))
    )
    core_half = lax.all_gather(chip_pair, "z", axis=0, tiled=True)
    other_half = lax.ppermute(core_half, "c", [(0, 1), (1, 0)])
    half_rows = core_half.shape[0]
    proj_cols = query_cols + 2 * kv_cols
    own_part = jnp.dot(
        gathered[:, :half_rows], core_half[:, :proj_cols], preferred_element_type=jnp.float32
    )
    own_part = lax.optimization_barrier(own_part)
    projected = own_part + jnp.dot(
        gathered[:, half_rows:], other_half[:, :proj_cols], preferred_element_type=jnp.float32
    )
    position = positions_of(segment)
    query_rows = rotate(
        projected[:, :query_cols].reshape(pack_rows, query_heads, HEAD), position
    ).astype(jnp.bfloat16)
    key_rows = rotate(
        projected[:, query_cols : query_cols + kv_cols].reshape(pack_rows, kv_heads, HEAD), position
    ).astype(jnp.bfloat16)
    value_rows = (
        projected[:, query_cols + kv_cols :].astype(jnp.bfloat16).reshape(pack_rows, kv_heads, HEAD)
    )
    cache_rows = jnp.concatenate([key_rows, value_rows], axis=-1)
    grouped_query = query_rows.reshape(pack_rows, kv_heads, group_size, HEAD)
    scores = (
        jnp.einsum("skgh,tkh->kgst", grouped_query, key_rows, preferred_element_type=jnp.float32)
        * score_scale
    )
    allowed = visible_pairs(segment, pack_rows)
    scores = jnp.where(allowed, scores, -1e30)
    row_max = jnp.max(scores, axis=-1, keepdims=True)
    weight = jnp.exp(scores - row_max)
    weight_sum = jnp.sum(weight, axis=-1)
    mixed_rows = (
        jnp.einsum(
            "kgst,tkh->kgsh",
            weight.astype(jnp.bfloat16),
            value_rows,
            preferred_element_type=jnp.float32,
        )
        / weight_sum[..., None]
    )
    attended = (
        jnp.transpose(mixed_rows, (2, 0, 1, 3)).astype(jnp.bfloat16).reshape(pack_rows, query_cols)
    )
    out_dims = (((1,), (1,)), ((), ()))
    out_rows = jnp.concatenate(
        (
            lax.dot_general(attended, core_half[:, proj_cols:], out_dims, preferred_element_type=jnp.float32),
            lax.dot_general(attended, other_half[:, proj_cols:], out_dims, preferred_element_type=jnp.float32),
        ),
        axis=1,
    )
    pieces = lax.all_to_all(
        out_rows.astype(jnp.bfloat16).reshape(tensor_size, -1, out_rows.shape[1]), "tensor", 0, 0, tiled=True
    )
    summed = jnp.sum(pieces.astype(jnp.float32), axis=0)
    split_s = summed.reshape(summed.shape[0], 2, -1, 2, packed_rows)
    split_s = lax.dynamic_slice_in_dim(jnp.concatenate((split_s, split_s), axis=1), core, 2, axis=1)
    split_s = lax.dynamic_slice_in_dim(jnp.concatenate((split_s, split_s), axis=3), pair_side, 2, axis=3)
    summed = jnp.transpose(split_s, (0, 2, 3, 1, 4)).reshape(summed.shape)
    hidden_out = (summed + rows_float).astype(jnp.bfloat16)
    return (hidden_out, cache_rows)


def solution(mesh):
    dp_size = mesh.shape["dp"]
    chip_mesh = Mesh(
        mesh.devices.reshape(dp_size // 4, 2, 2, mesh.shape["tensor"]), ("z", "xl", "c", "tensor")
    )
    dp = ("z", "xl", "c")
    return jax.shard_map(
        layer,
        mesh=chip_mesh,
        in_specs=(
            P((*dp, "tensor"), None),
            P(),
            P(dp, "tensor"),
            P(dp, "tensor"),
            P(dp, "tensor"),
            P("tensor", dp),
            P(dp),
        ),
        out_specs=(P((*dp, "tensor"), None), P(dp, "tensor", None)),
        check_vma=False,
    )
```
